512 devices in a mesh: dp: 32 (over z_lo, x), fly: 16 (over z_hi, y, core).
Axes of the slice: x: 4, y: 4, z: 16 (z_hi: 2, z_lo: 8; z = z_hi * 8 + z_lo), core: 2. Of those that a mesh axis runs over, the one named last changes fastest.
Arguments:
- tokens: bfloat16 [4096, 8192], P('dp', 'fly'), may hold values from -6 to 6
- hidden_grad: bfloat16 [4096, 16384], P('dp', 'fly'), may hold values from -6 to 6
- w_up: bfloat16 [6, 256, 16384], P(None, 'dp', 'fly'), may hold values from -0.15625 to 0.15625
- pattern: int32 [6, 64], P(None, 'fly'), may hold values 0 or 1
Outputs:
- input_grad: bfloat16 [4096, 8192], P('dp', 'fly')
- weight_grad: float32 [6, 256, 16384], P(None, 'dp', 'fly')
The draws below stay inside these ranges and needn't reach their ends.
Inputs may be any that keep to these rules, and one draw needn't show every extreme that they name: pattern[t, f] is 1 where block f of factor t is kept and 0 where it is dropped.
All inputs are finite; a program needn't handle non-finite values.
Results may differ from the reference program's by a relative error of at most 0.0049.
Values may be sent and summed in bfloat16 or wider, within the bound.
No kernel may reach another device: no remote copies, remote signals or barrier semaphores. Data moves between devices by JAX's collectives and lax.ppermute only.
A program may use at most 64 MiB of HBM per device.

```python
import jax
import jax.numpy as jnp
from jax import lax

BS = 256
SECTIONS = 6
D = 8192
FF = 16384
TOK_DEV = 128
REPLICAS = 32
TOKENS = 4096


def set_ends(drawn, stream_key, low, largest):
    place = [jax.random.randint(jax.random.fold_in(stream_key, axis), (), 0, length) for axis, length in enumerate(drawn.shape)]
    main_axis = drawn.shape.index(max(drawn.shape))
    beside = place[:main_axis] + [(place[main_axis] + 1) % drawn.shape[main_axis]] + place[main_axis + 1:]
    return drawn.at[tuple(place)].set(low).at[tuple(beside)].set(largest)


def block_scale(key, shape, cuts, low, largest):
    def one(axis_at, blocks):
        heights = jax.random.uniform(jax.random.fold_in(jax.random.fold_in(key, 6), axis_at), (blocks,), jnp.float32, low / len(cuts), largest / len(cuts))
        return jnp.repeat(jnp.exp(heights), shape[axis_at] // blocks).reshape((-1,) + (1,) * (len(shape) - axis_at - 1))

    level = one(*cuts[0])
    for cut in cuts[1:]:
        level = level * one(*cut)
    return level


def gaussian(own_key, shape, spread, most, shards=(), dtype=jnp.bfloat16):
    level = block_scale(own_key, shape, shards, -0.22, 0.18) if shards else 1.0
    array = jax.random.normal(own_key, shape, jnp.float32) * spread * level
    return jnp.minimum(jnp.maximum(array, -most), most).astype(dtype)


def setup_inputs(seed: int = 0) -> dict:
    splits = jax.random.split(jax.random.key(seed), 5)
    return {
        "tokens": gaussian(splits[0], (TOKENS, D), 1.0, 6.0, ((0, 32), (1, 16))),
        "hidden_grad": gaussian(splits[1], (TOKENS, FF), 1.0, 6.0, ((0, 32), (1, 16))),
        "w_up": gaussian(splits[2], (SECTIONS, BS, FF), (SECTIONS * BS) ** -0.5, 0.15625, ((1, 32), (2, 16))),
        "pattern": set_ends((jax.random.randint(splits[3], (SECTIONS, FF // BS), 0, 4) < 3).astype(jnp.int32), jax.random.fold_in(splits[3], 1), 0, 1),
    }


def flip_blocks(values, stride):
    if stride == 0:
        return values
    row_count, block_count, inner_size = values.shape
    shaped = values.reshape(row_count, block_count // (2 * stride), 2, stride, inner_size)
    return shaped[:, :, ::-1].reshape(row_count, block_count, inner_size)


def stride_of(factor):
    return 0 if factor == 0 else 2 ** (factor - 1)


def reference(tokens, hidden_grad, w_up, pattern):
    block_count = D // BS
    group_width = FF // block_count
    keep_cols = jnp.broadcast_to(pattern[:, :, None], (SECTIONS, FF // BS, BS)).reshape(SECTIONS, FF)
    masked = w_up * keep_cols.astype(jnp.bfloat16)[:, None, :]
    masked_f = masked.astype(jnp.float32).reshape(SECTIONS, BS, block_count, group_width)
    keep_f = keep_cols.astype(jnp.float32)
    token_sets = tokens.reshape(REPLICAS, TOK_DEV, D)
    grad_sets = hidden_grad.reshape(REPLICAS, TOK_DEV, FF)

    def replica_step(running, inputs_pair):
        token_rows, grad_rows = inputs_pair
        token_blocks = token_rows.astype(jnp.float32).reshape(TOK_DEV, block_count, BS)
        gathered = [flip_blocks(token_blocks, stride_of(factor)) for factor in range(SECTIONS)]
        pre_act = jnp.zeros((TOK_DEV, block_count, group_width), jnp.float32)
        for factor in range(SECTIONS):
            pre_act = pre_act + jnp.einsum("ngb,bgc->ngc", gathered[factor], masked_f[factor])
        squash = jax.nn.sigmoid(pre_act)
        derivative = squash * (1.0 + pre_act * (1.0 - squash))
        grad_pre = (grad_rows.astype(jnp.float32).reshape(TOK_DEV, block_count, group_width) * derivative).astype(jnp.bfloat16)
        grad_pre_f = grad_pre.astype(jnp.float32)
        input_total = jnp.zeros((TOK_DEV, block_count, BS), jnp.float32)
        updated = []
        for factor in range(SECTIONS):
            contrib = jnp.einsum("ngc,bgc->ngb", grad_pre_f, masked_f[factor])
            input_total = input_total + flip_blocks(contrib, stride_of(factor))
            product_term = jnp.einsum("ngb,ngc->bgc", gathered[factor], grad_pre_f).reshape(BS, FF)
            product_term = product_term * keep_f[factor][None, :]
            updated.append(running[factor] + product_term)
        return jnp.stack(updated), input_total.reshape(TOK_DEV, D).astype(jnp.bfloat16)

    initial = jnp.zeros((SECTIONS, BS, FF), jnp.float32)
    grad_total, input_rows = lax.scan(replica_step, initial, (token_sets, grad_sets))
    weight_grad = grad_total * (1.0 / REPLICAS)
    return input_rows.reshape(TOKENS, D), weight_grad
```

```python
import jax
import jax.numpy as jnp
from jax import lax
from jax.sharding import Mesh
from jax.sharding import PartitionSpec as P

BS = 256
ROWS = "zl"
COLS = "xx"
DP = (ROWS, COLS)


def partner_2(block, axis, bit):
    count = lax.axis_size(axis)
    route = []
    for low in range(count):
        high = low | 1 << bit
        if high != low and high < count:
            route += [(low, high), (high, low)]
    return lax.ppermute(block, axis, route)


def flip_blocks(values, stride):
    if stride == 0:
        return values
    row_count, block_count, inner_size = values.shape
    shaped = values.reshape(row_count, block_count // (2 * stride), 2, stride, inner_size)
    return shaped[:, :, ::-1].reshape(row_count, block_count, inner_size)


def stride_of(factor):
    return 0 if factor == 0 else 2 ** (factor - 1)


def gather_rows(w_up):
    inner = lax.all_gather(w_up, COLS, axis=1, tiled=True)
    return lax.all_gather(inner, ROWS, axis=1, tiled=True)


def scatter_rows(terms):
    rows, factor_count, width = terms.shape
    zl = lax.axis_size(ROWS)
    xx = lax.axis_size(COLS)
    part = lax.psum_scatter(terms.reshape(zl, rows // zl, factor_count, width), ROWS, scatter_dimension=0, tiled=True)
    part = lax.psum_scatter(part.reshape(xx, rows // (zl * xx), factor_count, width), COLS, scatter_dimension=0, tiled=True)
    return part.reshape(rows // (zl * xx), factor_count, width).transpose(1, 0, 2)


def body(tokens, hidden_grad, w_up, pattern):
    row_count, local_width = tokens.shape
    factor_count = w_up.shape[0]
    hidden_width = hidden_grad.shape[1]
    local_blocks = local_width // BS
    group_width = hidden_width // local_blocks
    weights = gather_rows(w_up)
    keep_cols = jnp.broadcast_to(pattern[:, :, None], (factor_count, pattern.shape[1], BS)).reshape(
        factor_count, hidden_width
    )
    masked = (weights * keep_cols.astype(jnp.bfloat16)[:, None, :]).reshape(
        factor_count, BS, local_blocks, group_width
    )
    keep_f = keep_cols.astype(jnp.float32)
    token_blocks = tokens.reshape(row_count, local_blocks, BS)
    gathered = []
    for factor in range(factor_count):
        stride = stride_of(factor)
        if stride < local_blocks:
            gathered.append(flip_blocks(token_blocks, stride))
        else:
            bit_number = (stride // local_blocks).bit_length() - 1
            partner = partner_2(tokens, "fly", bit_number)
            gathered.append(partner.reshape(row_count, local_blocks, BS))
    pre_act = jnp.zeros((row_count, local_blocks, group_width), jnp.float32)
    for factor in range(factor_count):
        pre_act = pre_act + jnp.einsum(
            "ngb,bgc->ngc", gathered[factor], masked[factor], preferred_element_type=jnp.float32
        )
    squash = jax.nn.sigmoid(pre_act)
    derivative = squash * (1.0 + pre_act * (1.0 - squash))
    grad_pre = (
        hidden_grad.reshape(row_count, local_blocks, group_width).astype(jnp.float32) * derivative
    ).astype(jnp.bfloat16)
    input_total = jnp.zeros((row_count, local_blocks, BS), jnp.float32)
    for factor in range(factor_count):
        stride = stride_of(factor)
        contrib = jnp.einsum(
            "ngc,bgc->ngb", grad_pre, masked[factor], preferred_element_type=jnp.float32
        )
        if stride < local_blocks:
            input_total = input_total + flip_blocks(contrib, stride)
        else:
            bit_number = (stride // local_blocks).bit_length() - 1
            returned = partner_2(contrib.reshape(row_count, local_width), "fly", bit_number)
            input_total = input_total + returned.reshape(row_count, local_blocks, BS)
    input_grad = input_total.reshape(row_count, local_width).astype(jnp.bfloat16)
    terms = []
    for factor in range(factor_count):
        product_term = jnp.einsum(
            "ngb,ngc->bgc", gathered[factor], grad_pre, preferred_element_type=jnp.float32
        )
        terms.append(product_term.reshape(BS, hidden_width) * keep_f[factor][None, :])
    summed = scatter_rows(jnp.stack(terms, axis=1))
    weight_grad = summed * (1.0 / (lax.axis_size(ROWS) * lax.axis_size(COLS)))
    return (input_grad, weight_grad)


def split_mesh(mesh):
    devices = mesh.devices
    xs = sorted({d.coords[0] for d in devices[:, 0]})
    cols = len(xs)
    return Mesh(devices.reshape(devices.shape[0] // cols, cols, devices.shape[1]), (ROWS, COLS, "fly"))


def solution(mesh):
    grid = split_mesh(mesh)
    return jax.shard_map(
        body,
        mesh=grid,
        in_specs=(P(DP, "fly"), P(DP, "fly"), P(None, DP, "fly"), P(None, "fly")),
        out_specs=(P(DP, "fly"), P(None, DP, "fly")),
        check_vma=False,
    )
```

```python
import jax
import jax.numpy as jnp
from jax import lax
from jax.sharding import Mesh
from jax.sharding import PartitionSpec as P

BS = 256
ROWS = "zl"
COLS = "xx"
DP = (ROWS, COLS)


def partner_2(block, axis, bit):
    count = lax.axis_size(axis)
    route = []
    for low in range(count):
        high = low | 1 << bit
        if high != low and high < count:
            route += [(low, high), (high, low)]
    return lax.ppermute(block, axis, route)


def flip_blocks(values, stride):
    if stride == 0:
        return values
    row_count, block_count, inner_size = values.shape
    shaped = values.reshape(row_count, block_count // (2 * stride), 2, stride, inner_size)
    return shaped[:, :, ::-1].reshape(row_count, block_count, inner_size)


def stride_of(factor):
    return 0 if factor == 0 else 2 ** (factor - 1)


def gather_rows(w_up):
    inner = lax.all_gather(w_up, COLS, axis=1, tiled=True)
    return lax.all_gather(inner, ROWS, axis=1, tiled=True)


def scatter_rows(terms):
    rows, factor_count, width = terms.shape
    zl = lax.axis_size(ROWS)
    xx = lax.axis_size(COLS)
    own = rows // (zl * xx)
    by_col = terms.reshape(zl, xx, own, factor_count, width).transpose(1, 0, 2, 3, 4)
    got = lax.all_to_all(by_col.astype(jnp.bfloat16), COLS, 0, 0, tiled=True)
    part = got.astype(jnp.float32).reshape(xx, zl, own, factor_count, width).sum(0)
    got = lax.all_to_all(part.astype(jnp.bfloat16), ROWS, 0, 0, tiled=True)
    part = got.astype(jnp.float32).reshape(zl, own, factor_count, width).sum(0)
    return part.transpose(1, 0, 2)


def body(tokens, hidden_grad, w_up, pattern):
    row_count, local_width = tokens.shape
    factor_count = w_up.shape[0]
    hidden_width = hidden_grad.shape[1]
    local_blocks = local_width // BS
    group_width = hidden_width // local_blocks
    weights = gather_rows(w_up)
    keep_cols = jnp.broadcast_to(pattern[:, :, None], (factor_count, pattern.shape[1], BS)).reshape(
        factor_count, hidden_width
    )
    masked = (weights * keep_cols.astype(jnp.bfloat16)[:, None, :]).reshape(
        factor_count, BS, local_blocks, group_width
    )
    keep_f = keep_cols.astype(jnp.float32)
    token_blocks = tokens.reshape(row_count, local_blocks, BS)
    gathered = []
    for factor in range(factor_count):
        stride = stride_of(factor)
        if stride < local_blocks:
            gathered.append(flip_blocks(token_blocks, stride))
        else:
            bit_number = (stride // local_blocks).bit_length() - 1
            partner = partner_2(tokens, "fly", bit_number)
            gathered.append(partner.reshape(row_count, local_blocks, BS))
    pre_act = jnp.zeros((row_count, local_blocks, group_width), jnp.float32)
    for factor in range(factor_count):
        pre_act = pre_act + jnp.einsum(
            "ngb,bgc->ngc", gathered[factor], masked[factor], preferred_element_type=jnp.float32
        )
    squash = jax.nn.sigmoid(pre_act)
    derivative = squash * (1.0 + pre_act * (1.0 - squash))
    grad_pre = (
        hidden_grad.reshape(row_count, local_blocks, group_width).astype(jnp.float32) * derivative
    ).astype(jnp.bfloat16)
    input_total = jnp.zeros((row_count, local_blocks, BS), jnp.float32)
    for factor in range(factor_count):
        stride = stride_of(factor)
        contrib = jnp.einsum(
            "ngc,bgc->ngb", grad_pre, masked[factor], preferred_element_type=jnp.float32
        )
        if stride < local_blocks:
            input_total = input_total + flip_blocks(contrib, stride)
        else:
            bit_number = (stride // local_blocks).bit_length() - 1
            returned = partner_2(contrib.reshape(row_count, local_width), "fly", bit_number)
            input_total = input_total + returned.reshape(row_count, local_blocks, BS)
    input_grad = input_total.reshape(row_count, local_width).astype(jnp.bfloat16)
    terms = []
    for factor in range(factor_count):
        product_term = jnp.einsum(
            "ngb,ngc->bgc", gathered[factor], grad_pre, preferred_element_type=jnp.float32
        )
        terms.append(product_term.reshape(BS, hidden_width) * keep_f[factor][None, :])
    summed = scatter_rows(jnp.stack(terms, axis=1))
    weight_grad = summed * (1.0 / (lax.axis_size(ROWS) * lax.axis_size(COLS)))
    return (input_grad, weight_grad)


def split_mesh(mesh):
    devices = mesh.devices
    xs = sorted({d.coords[0] for d in devices[:, 0]})
    cols = len(xs)
    return Mesh(devices.reshape(devices.shape[0] // cols, cols, devices.shape[1]), (ROWS, COLS, "fly"))


def solution(mesh):
    grid = split_mesh(mesh)
    return jax.shard_map(
        body,
        mesh=grid,
        in_specs=(P(DP, "fly"), P(DP, "fly"), P(None, DP, "fly"), P(None, "fly")),
        out_specs=(P(DP, "fly"), P(None, DP, "fly")),
        check_vma=False,
    )
```

```python
import jax
import jax.numpy as jnp
from jax import lax
from jax.sharding import Mesh
from jax.sharding import PartitionSpec as P

BS = 256
ROWS = "zl"
COLS = "xx"
DP = (ROWS, COLS)


def partner_2(block, axis, bit):
    count = lax.axis_size(axis)
    route = []
    for low in range(count):
        high = low | 1 << bit
        if high != low and high < count:
            route += [(low, high), (high, low)]
    return lax.ppermute(block, axis, route)


def flip_blocks(values, stride):
    if stride == 0:
        return values
    row_count, block_count, inner_size = values.shape
    shaped = values.reshape(row_count, block_count // (2 * stride), 2, stride, inner_size)
    return shaped[:, :, ::-1].reshape(row_count, block_count, inner_size)


def stride_of(factor):
    return 0 if factor == 0 else 2 ** (factor - 1)


def gather_rows(w_up):
    inner = lax.all_gather(w_up, COLS, axis=1, tiled=True)
    return lax.all_gather(inner, ROWS, axis=1, tiled=True)


def scatter_rows(terms):
    xx, zl, own, factor_count, width = terms.shape
    got = lax.all_to_all(terms, COLS, 0, 0, tiled=True)
    part = got.astype(jnp.float32).sum(0)
    got = lax.all_to_all(part.astype(jnp.bfloat16), ROWS, 0, 0, tiled=True)
    part = got.astype(jnp.float32).sum(0)
    return part.transpose(1, 0, 2)


def body(tokens, hidden_grad, w_up, pattern):
    row_count, local_width = tokens.shape
    factor_count = w_up.shape[0]
    hidden_width = hidden_grad.shape[1]
    local_blocks = local_width // BS
    group_width = hidden_width // local_blocks
    zl = lax.axis_size(ROWS)
    xx = lax.axis_size(COLS)
    own = BS // (zl * xx)
    weights = gather_rows(w_up)
    keep_cols = jnp.broadcast_to(pattern[:, :, None], (factor_count, pattern.shape[1], BS)).reshape(
        factor_count, hidden_width
    )
    masked = (weights * keep_cols.astype(jnp.bfloat16)[:, None, :]).reshape(
        factor_count, BS, local_blocks, group_width
    )
    keep_f = keep_cols.astype(jnp.float32).reshape(factor_count, local_blocks, group_width)
    token_blocks = tokens.reshape(row_count, local_blocks, BS)
    gathered = []
    for factor in range(factor_count):
        stride = stride_of(factor)
        if stride < local_blocks:
            gathered.append(flip_blocks(token_blocks, stride))
        else:
            bit_number = (stride // local_blocks).bit_length() - 1
            partner = partner_2(tokens, "fly", bit_number)
            gathered.append(partner.reshape(row_count, local_blocks, BS))
    reads = jnp.stack(gathered, axis=2)
    grads = []
    contribs = []
    products = []
    for group in range(local_blocks):
        lhs = reads[:, group].reshape(row_count, factor_count * BS)
        rhs = masked[:, :, group, :].reshape(factor_count * BS, group_width)
        pre_act = jnp.dot(lhs, rhs, preferred_element_type=jnp.float32)
        squash = jax.nn.sigmoid(pre_act)
        derivative = squash * (1.0 + pre_act * (1.0 - squash))
        grad_pre = (hidden_grad[:, group * group_width:(group + 1) * group_width].astype(jnp.float32) * derivative).astype(
            jnp.bfloat16
        )
        contribs.append(
            lax.dot_general(grad_pre, rhs, (((1,), (1,)), ((), ())), preferred_element_type=jnp.float32).reshape(
                row_count, factor_count, BS
            )
        )
        cols = reads[:, group].reshape(row_count, factor_count, zl, xx, own).transpose(0, 3, 2, 4, 1)
        products.append(
            lax.dot_general(
                cols.reshape(row_count, BS * factor_count), grad_pre, (((0,), (0,)), ((), ())),
                preferred_element_type=jnp.float32,
            ).reshape(xx, zl, own, factor_count, group_width)
        )
    contrib_all = jnp.stack(contribs, axis=1)
    input_total = jnp.zeros((row_count, local_blocks, BS), jnp.float32)
    for factor in range(factor_count):
        stride = stride_of(factor)
        contrib = contrib_all[:, :, factor, :]
        if stride < local_blocks:
            input_total = input_total + flip_blocks(contrib, stride)
        else:
            bit_number = (stride // local_blocks).bit_length() - 1
            returned = partner_2(contrib.reshape(row_count, local_width), "fly", bit_number)
            input_total = input_total + returned.reshape(row_count, local_blocks, BS)
    input_grad = input_total.reshape(row_count, local_width).astype(jnp.bfloat16)
    terms = jnp.stack(products, axis=4) * keep_f[None, None, None]
    summed = scatter_rows(terms.reshape(xx, zl, own, factor_count, hidden_width).astype(jnp.bfloat16))
    weight_grad = summed * (1.0 / (zl * xx))
    return (input_grad, weight_grad)


def split_mesh(mesh):
    devices = mesh.devices
    xs = sorted({d.coords[0] for d in devices[:, 0]})
    cols = len(xs)
    return Mesh(devices.reshape(devices.shape[0] // cols, cols, devices.shape[1]), (ROWS, COLS, "fly"))


def solution(mesh):
    grid = split_mesh(mesh)
    return jax.shard_map(
        body,
        mesh=grid,
        in_specs=(P(DP, "fly"), P(DP, "fly"), P(None, DP, "fly"), P(None, "fly")),
        out_specs=(P(DP, "fly"), P(None, DP, "fly")),
        check_vma=False,
    )
```

```python
import jax
import jax.numpy as jnp
from jax import lax
from jax.sharding import Mesh
from jax.sharding import PartitionSpec as P

BS = 256
ROWS = "zl"
COLS = "xx"
DP = (ROWS, COLS)


def partner_2(block, axis, bit):
    count = lax.axis_size(axis)
    route = []
    for low in range(count):
        high = low | 1 << bit
        if high != low and high < count:
            route += [(low, high), (high, low)]
    return lax.ppermute(block, axis, route)


def flip_blocks(values, stride):
    if stride == 0:
        return values
    row_count, block_count, inner_size = values.shape
    shaped = values.reshape(row_count, block_count // (2 * stride), 2, stride, inner_size)
    return shaped[:, :, ::-1].reshape(row_count, block_count, inner_size)


def stride_of(factor):
    return 0 if factor == 0 else 2 ** (factor - 1)


def gather_rows(w_up):
    inner = lax.all_gather(w_up, COLS, axis=1, tiled=True)
    return lax.all_gather(inner, ROWS, axis=1, tiled=True)


def scatter_rows(terms):
    xx, zl, own, factor_count, width = terms.shape
    got = lax.all_to_all(terms, COLS, 0, 0, tiled=True)
    part = got.astype(jnp.float32).sum(0)
    got = lax.all_to_all(part.astype(jnp.bfloat16), ROWS, 0, 0, tiled=True)
    part = got.astype(jnp.float32).sum(0)
    return part.transpose(1, 0, 2)


def body(tokens, hidden_grad, w_up, pattern):
    row_count, local_width = tokens.shape
    factor_count = w_up.shape[0]
    hidden_width = hidden_grad.shape[1]
    local_blocks = local_width // BS
    group_width = hidden_width // local_blocks
    zl = lax.axis_size(ROWS)
    xx = lax.axis_size(COLS)
    own = BS // (zl * xx)
    keep_cols = jnp.broadcast_to(pattern[:, :, None], (factor_count, pattern.shape[1], BS)).reshape(
        factor_count, local_blocks, group_width
    )
    token_blocks = tokens.reshape(row_count, local_blocks, BS)
    gathered = []
    for factor in range(factor_count):
        stride = stride_of(factor)
        if stride < local_blocks:
            gathered.append(flip_blocks(token_blocks, stride))
        else:
            bit_number = (stride // local_blocks).bit_length() - 1
            partner = partner_2(tokens, "fly", bit_number)
            gathered.append(partner.reshape(row_count, local_blocks, BS))
    reads = jnp.stack(gathered, axis=2)
    contribs = []
    sums = []
    for group in range(local_blocks):
        weights = gather_rows(w_up[:, :, group * group_width:(group + 1) * group_width])
        rhs = (weights * keep_cols[:, group].astype(jnp.bfloat16)[:, None, :]).reshape(factor_count * BS, group_width)
        lhs = reads[:, group].reshape(row_count, factor_count * BS)
        pre_act = jnp.dot(lhs, rhs, preferred_element_type=jnp.float32)
        squash = jax.nn.sigmoid(pre_act)
        derivative = squash * (1.0 + pre_act * (1.0 - squash))
        grad_pre = (hidden_grad[:, group * group_width:(group + 1) * group_width].astype(jnp.float32) * derivative).astype(
            jnp.bfloat16
        )
        contribs.append(
            lax.dot_general(grad_pre, rhs, (((1,), (1,)), ((), ())), preferred_element_type=jnp.float32).reshape(
                row_count, factor_count, BS
            )
        )
        cols = reads[:, group].reshape(row_count, factor_count, zl, xx, own).transpose(0, 3, 2, 4, 1)
        product = lax.dot_general(
            cols.reshape(row_count, BS * factor_count), grad_pre, (((0,), (0,)), ((), ())),
            preferred_element_type=jnp.float32,
        ).reshape(xx, zl, own, factor_count, group_width)
        product = product * keep_cols[:, group].astype(jnp.float32)[None, None, None]
        sums.append(scatter_rows(product.astype(jnp.bfloat16)))
    contrib_all = jnp.stack(contribs, axis=1)
    input_total = jnp.zeros((row_count, local_blocks, BS), jnp.float32)
    for factor in range(factor_count):
        stride = stride_of(factor)
        contrib = contrib_all[:, :, factor, :]
        if stride < local_blocks:
            input_total = input_total + flip_blocks(contrib, stride)
        else:
            bit_number = (stride // local_blocks).bit_length() - 1
            returned = partner_2(contrib.reshape(row_count, local_width), "fly", bit_number)
            input_total = input_total + returned.reshape(row_count, local_blocks, BS)
    input_grad = input_total.reshape(row_count, local_width).astype(jnp.bfloat16)
    weight_grad = jnp.concatenate(sums, axis=2) * (1.0 / (zl * xx))
    return (input_grad, weight_grad)


def split_mesh(mesh):
    devices = mesh.devices
    xs = sorted({d.coords[0] for d in devices[:, 0]})
    cols = len(xs)
    return Mesh(devices.reshape(devices.shape[0] // cols, cols, devices.shape[1]), (ROWS, COLS, "fly"))


def solution(mesh):
    grid = split_mesh(mesh)
    return jax.shard_map(
        body,
        mesh=grid,
        in_specs=(P(DP, "fly"), P(DP, "fly"), P(None, DP, "fly"), P(None, "fly")),
        out_specs=(P(DP, "fly"), P(None, DP, "fly")),
        check_vma=False,
    )
```

```python
import jax
import jax.numpy as jnp
from jax import lax
from jax.sharding import Mesh
from jax.sharding import PartitionSpec as P

BS = 256
ROWS = "zl"
COLS = "xx"
DP = (ROWS, COLS)


def partner_2(block, axis, bit):
    count = lax.axis_size(axis)
    route = []
    for low in range(count):
        high = low | 1 << bit
        if high != low and high < count:
            route += [(low, high), (high, low)]
    return lax.ppermute(block, axis, route)


def flip_blocks(values, stride):
    if stride == 0:
        return values
    row_count, block_count, inner_size = values.shape
    shaped = values.reshape(row_count, block_count // (2 * stride), 2, stride, inner_size)
    return shaped[:, :, ::-1].reshape(row_count, block_count, inner_size)


def stride_of(factor):
    return 0 if factor == 0 else 2 ** (factor - 1)


def gather_rows(w_up):
    factor_count, own, width = w_up.shape
    zl = lax.axis_size(ROWS)
    xx = lax.axis_size(COLS)
    copies = jnp.broadcast_to(w_up[None], (zl, factor_count, own, width))
    by_row = lax.all_to_all(copies, ROWS, 0, 0, tiled=True)
    copies = jnp.broadcast_to(by_row[None], (xx, zl, factor_count, own, width))
    both = lax.all_to_all(copies, COLS, 0, 0, tiled=True)
    return both.transpose(2, 1, 0, 3, 4).reshape(factor_count, zl * xx * own, width)


def scatter_rows(terms):
    xx, zl, own, factor_count, width = terms.shape
    got = lax.all_to_all(terms, COLS, 0, 0, tiled=True)
    part = got.astype(jnp.float32).sum(0)
    got = lax.all_to_all(part.astype(jnp.bfloat16), ROWS, 0, 0, tiled=True)
    part = got.astype(jnp.float32).sum(0)
    return part.transpose(1, 0, 2)


def body(tokens, hidden_grad, w_up, pattern):
    row_count, local_width = tokens.shape
    factor_count = w_up.shape[0]
    hidden_width = hidden_grad.shape[1]
    local_blocks = local_width // BS
    group_width = hidden_width // local_blocks
    zl = lax.axis_size(ROWS)
    xx = lax.axis_size(COLS)
    own = BS // (zl * xx)
    weights = gather_rows(w_up)
    keep_cols = jnp.broadcast_to(pattern[:, :, None], (factor_count, pattern.shape[1], BS)).reshape(
        factor_count, hidden_width
    )
    masked = (weights * keep_cols.astype(jnp.bfloat16)[:, None, :]).reshape(
        factor_count, BS, local_blocks, group_width
    )
    keep_f = keep_cols.astype(jnp.float32).reshape(factor_count, local_blocks, group_width)
    token_blocks = tokens.reshape(row_count, local_blocks, BS)
    gathered = []
    for factor in range(factor_count):
        stride = stride_of(factor)
        if stride < local_blocks:
            gathered.append(flip_blocks(token_blocks, stride))
        else:
            bit_number = (stride // local_blocks).bit_length() - 1
            partner = partner_2(tokens, "fly", bit_number)
            gathered.append(partner.reshape(row_count, local_blocks, BS))
    reads = jnp.stack(gathered, axis=2)
    grads = []
    contribs = []
    products = []
    for group in range(local_blocks):
        lhs = reads[:, group].reshape(row_count, factor_count * BS)
        rhs = masked[:, :, group, :].reshape(factor_count * BS, group_width)
        pre_act = jnp.dot(lhs, rhs, preferred_element_type=jnp.float32)
        squash = jax.nn.sigmoid(pre_act)
        derivative = squash * (1.0 + pre_act * (1.0 - squash))
        grad_pre = (hidden_grad[:, group * group_width:(group + 1) * group_width].astype(jnp.float32) * derivative).astype(
            jnp.bfloat16
        )
        contribs.append(
            lax.dot_general(grad_pre, rhs, (((1,), (1,)), ((), ())), preferred_element_type=jnp.float32).reshape(
                row_count, factor_count, BS
            )
        )
        cols = reads[:, group].reshape(row_count, factor_count, zl, xx, own).transpose(0, 3, 2, 4, 1)
        products.append(
            lax.dot_general(
                cols.reshape(row_count, BS * factor_count), grad_pre, (((0,), (0,)), ((), ())),
                preferred_element_type=jnp.float32,
            ).reshape(xx, zl, own, factor_count, group_width)
        )
    contrib_all = jnp.stack(contribs, axis=1)
    input_total = jnp.zeros((row_count, local_blocks, BS), jnp.float32)
    for factor in range(factor_count):
        stride = stride_of(factor)
        contrib = contrib_all[:, :, factor, :]
        if stride < local_blocks:
            input_total = input_total + flip_blocks(contrib, stride)
        else:
            bit_number = (stride // local_blocks).bit_length() - 1
            returned = partner_2(contrib.reshape(row_count, local_width), "fly", bit_number)
            input_total = input_total + returned.reshape(row_count, local_blocks, BS)
    input_grad = input_total.reshape(row_count, local_width).astype(jnp.bfloat16)
    terms = jnp.stack(products, axis=4) * keep_f[None, None, None]
    summed = scatter_rows(terms.reshape(xx, zl, own, factor_count, hidden_width).astype(jnp.bfloat16))
    weight_grad = summed * (1.0 / (zl * xx))
    return (input_grad, weight_grad)


def split_mesh(mesh):
    devices = mesh.devices
    xs = sorted({d.coords[0] for d in devices[:, 0]})
    cols = len(xs)
    return Mesh(devices.reshape(devices.shape[0] // cols, cols, devices.shape[1]), (ROWS, COLS, "fly"))


def solution(mesh):
    grid = split_mesh(mesh)
    return jax.shard_map(
        body,
        mesh=grid,
        in_specs=(P(DP, "fly"), P(DP, "fly"), P(None, DP, "fly"), P(None, "fly")),
        out_specs=(P(DP, "fly"), P(None, DP, "fly")),
        check_vma=False,
    )
```

```python
import jax
import jax.numpy as jnp
from jax import lax
from jax.sharding import Mesh
from jax.sharding import PartitionSpec as P


BS = 256
ROWS = "zl"
COLS = "xx"
DP = (ROWS, COLS)


def partner_2(block, axis, bit):
    count = lax.axis_size(axis)
    route = []
    for low in range(count):
        high = low | 1 << bit
        if high != low and high < count:
            route += [(low, high), (high, low)]
    return lax.ppermute(block, axis, route)


def flip_blocks(values, stride):
    if stride == 0:
        return values
    row_count, block_count, inner_size = values.shape
    shaped = values.reshape(row_count, block_count // (2 * stride), 2, stride, inner_size)
    return shaped[:, :, ::-1].reshape(row_count, block_count, inner_size)


def stride_of(factor):
    return 0 if factor == 0 else 2 ** (factor - 1)


def gather_rows(w_up):
    factor_count, own, width = w_up.shape
    zl = lax.axis_size(ROWS)
    xx = lax.axis_size(COLS)
    copies = jnp.broadcast_to(w_up[None], (zl, factor_count, own, width))
    by_row = lax.all_to_all(copies, ROWS, 0, 0, tiled=True)
    copies = jnp.broadcast_to(by_row[None], (xx, zl, factor_count, own, width))
    both = lax.all_to_all(copies, COLS, 0, 0, tiled=True)
    return both.transpose(2, 1, 0, 3, 4).reshape(factor_count, zl * xx * own, width)


def scatter_rows(terms):
    got = lax.all_to_all(terms, COLS, 0, 0, tiled=True)
    part = got.astype(jnp.float32).sum(0)
    got = lax.all_to_all(part.astype(jnp.bfloat16), ROWS, 0, 0, tiled=True)
    part = got.astype(jnp.float32).sum(0)
    return part.transpose(1, 0, 2)


def layer(tokens, hidden_grad, w_up, pattern):
    row_count, local_width = tokens.shape
    factor_count = w_up.shape[0]
    hidden_width = hidden_grad.shape[1]
    local_blocks = local_width // BS
    group_width = hidden_width // local_blocks
    zl = lax.axis_size(ROWS)
    xx = lax.axis_size(COLS)
    own = BS // (zl * xx)
    weights = gather_rows(w_up)
    keep_cols = jnp.broadcast_to(pattern[:, :, None], (factor_count, pattern.shape[1], BS)).reshape(
        factor_count, hidden_width
    )
    masked = (weights * keep_cols.astype(jnp.bfloat16)[:, None, :]).reshape(
        factor_count, BS, local_blocks, group_width
    )
    keep_f = keep_cols.astype(jnp.float32).reshape(factor_count, local_blocks, group_width)
    token_blocks = tokens.reshape(row_count, local_blocks, BS)
    gathered = []
    for factor in range(factor_count):
        stride = stride_of(factor)
        if stride < local_blocks:
            gathered.append(flip_blocks(token_blocks, stride))
        else:
            bit_number = (stride // local_blocks).bit_length() - 1
            partner = partner_2(tokens, "fly", bit_number)
            gathered.append(partner.reshape(row_count, local_blocks, BS))
    reads = jnp.stack(gathered, axis=2)
    contribs = []
    products = []
    for group in range(local_blocks):
        lhs = reads[:, group].reshape(row_count, factor_count * BS)
        rhs = masked[:, :, group, :].reshape(factor_count * BS, group_width)
        pre_act = jnp.dot(lhs, rhs, preferred_element_type=jnp.float32)
        squash = jax.nn.sigmoid(pre_act)
        derivative = squash * (1.0 + pre_act * (1.0 - squash))
        grad_pre = (hidden_grad[:, group * group_width:(group + 1) * group_width].astype(jnp.float32) * derivative).astype(
            jnp.bfloat16
        )
        contribs.append(
            lax.dot_general(grad_pre, rhs, (((1,), (1,)), ((), ())), preferred_element_type=jnp.float32).reshape(
                row_count, factor_count, BS
            )
        )
        cols = reads[:, group].reshape(row_count, factor_count, zl, xx, own).transpose(0, 3, 2, 4, 1)
        products.append(
            lax.dot_general(
                cols.reshape(row_count, BS * factor_count), grad_pre, (((0,), (0,)), ((), ())),
                preferred_element_type=jnp.float32,
            ).reshape(xx, zl, own, factor_count, group_width)
        )
    contrib_all = jnp.stack(contribs, axis=1)
    input_total = jnp.zeros((row_count, local_blocks, BS), jnp.float32)
    for factor in range(factor_count):
        stride = stride_of(factor)
        contrib = contrib_all[:, :, factor, :]
        if stride < local_blocks:
            input_total = input_total + flip_blocks(contrib, stride)
        else:
            bit_number = (stride // local_blocks).bit_length() - 1
            returned = partner_2(contrib.reshape(row_count, local_width), "fly", bit_number)
            input_total = input_total + returned.reshape(row_count, local_blocks, BS)
    input_grad = input_total.reshape(row_count, local_width).astype(jnp.bfloat16)
    terms = jnp.stack(products, axis=4) * keep_f[None, None, None]
    summed = scatter_rows(terms.reshape(xx, zl, own, factor_count, hidden_width).astype(jnp.bfloat16))
    weight_grad = summed * (1.0 / (zl * xx))
    return (input_grad, weight_grad)


def split_mesh(mesh):
    devices = mesh.devices
    xs = sorted({d.coords[0] for d in devices[:, 0]})
    cols = len(xs)
    return Mesh(devices.reshape(devices.shape[0] // cols, cols, devices.shape[1]), (ROWS, COLS, "fly"))


def solution(mesh):
    grid = split_mesh(mesh)
    return jax.shard_map(
        layer,
        mesh=grid,
        in_specs=(P(DP, "fly"), P(DP, "fly"), P(None, DP, "fly"), P(None, "fly")),
        out_specs=(P(DP, "fly"), P(None, DP, "fly")),
        check_vma=False,
    )
```

```python
import jax
import jax.numpy as jnp
from jax import lax
from jax.sharding import Mesh
from jax.sharding import PartitionSpec as P


BS = 256
ROWS = "zl"
COLS = "xx"
DP = (ROWS, COLS)


def partner_2(block, axis, bit):
    count = lax.axis_size(axis)
    route = []
    for low in range(count):
        high = low | 1 << bit
        if high != low and high < count:
            route += [(low, high), (high, low)]
    return lax.ppermute(block, axis, route)


def flip_blocks(values, stride):
    if stride == 0:
        return values
    row_count, block_count, inner_size = values.shape
    shaped = values.reshape(row_count, block_count // (2 * stride), 2, stride, inner_size)
    return shaped[:, :, ::-1].reshape(row_count, block_count, inner_size)


def stride_of(factor):
    return 0 if factor == 0 else 2 ** (factor - 1)


def gather_line(block, axis):
    count = lax.axis_size(axis)
    bits = count.bit_length() - 1
    assert 1 << bits == count
    place = lax.axis_index(axis)
    held = block[None]
    for step in range(bits):
        dist = count >> (step + 1)
        got = lax.ppermute(held, axis, [(i, i ^ dist) for i in range(count)])
        upper = (place & dist) != 0
        held = jnp.where(upper, jnp.stack([got, held]), jnp.stack([held, got]))
    order = tuple(reversed(range(bits))) + tuple(range(bits, bits + block.ndim))
    return held.reshape((2,) * bits + block.shape).transpose(order).reshape((count,) + block.shape)


def gather_rows(w_up):
    factor_count, own, width = w_up.shape
    zl = lax.axis_size(ROWS)
    xx = lax.axis_size(COLS)
    by_row = gather_line(w_up, ROWS)
    copies = jnp.broadcast_to(by_row[None], (xx, zl, factor_count, own, width))
    both = lax.all_to_all(copies, COLS, 0, 0, tiled=True)
    return both.transpose(2, 1, 0, 3, 4).reshape(factor_count, zl * xx * own, width)


def scatter_rows(terms):
    got = lax.all_to_all(terms, COLS, 0, 0, tiled=True)
    part = got.astype(jnp.float32).sum(0)
    got = lax.all_to_all(part.astype(jnp.bfloat16), ROWS, 0, 0, tiled=True)
    part = got.astype(jnp.float32).sum(0)
    return part.transpose(1, 0, 2)


def layer(tokens, hidden_grad, w_up, pattern):
    row_count, local_width = tokens.shape
    factor_count = w_up.shape[0]
    hidden_width = hidden_grad.shape[1]
    local_blocks = local_width // BS
    group_width = hidden_width // local_blocks
    zl = lax.axis_size(ROWS)
    xx = lax.axis_size(COLS)
    own = BS // (zl * xx)
    keep_cols = jnp.broadcast_to(pattern[:, :, None], (factor_count, pattern.shape[1], BS)).reshape(
        factor_count, local_blocks, group_width
    )
    token_blocks = tokens.reshape(row_count, local_blocks, BS)
    gathered = []
    for factor in range(factor_count):
        stride = stride_of(factor)
        if stride < local_blocks:
            gathered.append(flip_blocks(token_blocks, stride))
        else:
            bit_number = (stride // local_blocks).bit_length() - 1
            partner = partner_2(tokens, "fly", bit_number)
            gathered.append(partner.reshape(row_count, local_blocks, BS))
    reads = jnp.stack(gathered, axis=2)
    contribs = []
    sums = []
    for group in range(local_blocks):
        weights = gather_rows(w_up[:, :, group * group_width:(group + 1) * group_width])
        rhs = (weights * keep_cols[:, group].astype(jnp.bfloat16)[:, None, :]).reshape(factor_count * BS, group_width)
        lhs = reads[:, group].reshape(row_count, factor_count * BS)
        pre_act = jnp.dot(lhs, rhs, preferred_element_type=jnp.float32)
        squash = jax.nn.sigmoid(pre_act)
        derivative = squash * (1.0 + pre_act * (1.0 - squash))
        grad_pre = (hidden_grad[:, group * group_width:(group + 1) * group_width].astype(jnp.float32) * derivative).astype(
            jnp.bfloat16
        )
        contribs.append(
            lax.dot_general(grad_pre, rhs, (((1,), (1,)), ((), ())), preferred_element_type=jnp.float32).reshape(
                row_count, factor_count, BS
            )
        )
        cols = reads[:, group].reshape(row_count, factor_count, zl, xx, own).transpose(0, 3, 2, 4, 1)
        product = lax.dot_general(
            cols.reshape(row_count, BS * factor_count), grad_pre, (((0,), (0,)), ((), ())),
            preferred_element_type=jnp.float32,
        ).reshape(xx, zl, own, factor_count, group_width)
        product = product * keep_cols[:, group].astype(jnp.float32)[None, None, None]
        sums.append(scatter_rows(product.astype(jnp.bfloat16)))
    contrib_all = jnp.stack(contribs, axis=1)
    input_total = jnp.zeros((row_count, local_blocks, BS), jnp.float32)
    for factor in range(factor_count):
        stride = stride_of(factor)
        contrib = contrib_all[:, :, factor, :]
        if stride < local_blocks:
            input_total = input_total + flip_blocks(contrib, stride)
        else:
            bit_number = (stride // local_blocks).bit_length() - 1
            returned = partner_2(contrib.reshape(row_count, local_width), "fly", bit_number)
            input_total = input_total + returned.reshape(row_count, local_blocks, BS)
    input_grad = input_total.reshape(row_count, local_width).astype(jnp.bfloat16)
    weight_grad = jnp.concatenate(sums, axis=2) * (1.0 / (zl * xx))
    return (input_grad, weight_grad)


def split_mesh(mesh):
    devices = mesh.devices
    xs = sorted({d.coords[0] for d in devices[:, 0]})
    cols = len(xs)
    return Mesh(devices.reshape(devices.shape[0] // cols, cols, devices.shape[1]), (ROWS, COLS, "fly"))


def solution(mesh):
    grid = split_mesh(mesh)
    return jax.shard_map(
        layer,
        mesh=grid,
        in_specs=(P(DP, "fly"), P(DP, "fly"), P(None, DP, "fly"), P(None, "fly")),
        out_specs=(P(DP, "fly"), P(None, DP, "fly")),
        check_vma=False,
    )
```

```python
import jax
import jax.numpy as jnp
from jax import lax
from jax.sharding import Mesh
from jax.sharding import PartitionSpec as P


BS = 256
ROWS = "zl"
COLS = "xx"
DP = (ROWS, COLS)


def partner_2(block, axis, bit):
    count = lax.axis_size(axis)
    route = []
    for low in range(count):
        high = low | 1 << bit
        if high != low and high < count:
            route += [(low, high), (high, low)]
    return lax.ppermute(block, axis, route)


def flip_blocks(values, stride):
    if stride == 0:
        return values
    row_count, block_count, inner_size = values.shape
    shaped = values.reshape(row_count, block_count // (2 * stride), 2, stride, inner_size)
    return shaped[:, :, ::-1].reshape(row_count, block_count, inner_size)


def stride_of(factor):
    return 0 if factor == 0 else 2 ** (factor - 1)


def gather_line(block, axis):
    count = lax.axis_size(axis)
    bits = count.bit_length() - 1
    assert 1 << bits == count
    place = lax.axis_index(axis)
    held = block[None]
    for step in range(bits):
        dist = count >> (step + 1)
        got = lax.ppermute(held, axis, [(i, i ^ dist) for i in range(count)])
        upper = (place & dist) != 0
        held = jnp.where(upper, jnp.stack([got, held]), jnp.stack([held, got]))
    order = tuple(reversed(range(bits))) + tuple(range(bits, bits + block.ndim))
    return held.reshape((2,) * bits + block.shape).transpose(order).reshape((count,) + block.shape)


def gather_rows(w_up):
    factor_count, own, width = w_up.shape
    zl = lax.axis_size(ROWS)
    xx = lax.axis_size(COLS)
    by_row = gather_line(w_up, ROWS)
    copies = jnp.broadcast_to(by_row[None], (xx, zl, factor_count, own, width))
    both = lax.all_to_all(copies, COLS, 0, 0, tiled=True)
    return both.transpose(2, 1, 0, 3, 4).reshape(factor_count, zl * xx * own, width)


def scatter_rows(terms):
    got = lax.all_to_all(terms, COLS, 0, 0, tiled=True)
    part = got.astype(jnp.float32).sum(0)
    got = lax.all_to_all(part.astype(jnp.bfloat16), ROWS, 0, 0, tiled=True)
    part = got.astype(jnp.float32).sum(0)
    return part.transpose(1, 0, 2)


def layer(tokens, hidden_grad, w_up, pattern):
    row_count, local_width = tokens.shape
    factor_count = w_up.shape[0]
    hidden_width = hidden_grad.shape[1]
    local_blocks = local_width // BS
    group_width = hidden_width // local_blocks
    zl = lax.axis_size(ROWS)
    xx = lax.axis_size(COLS)
    own = BS // (zl * xx)
    half = w_up.shape[2] // 2
    weights = jnp.concatenate([gather_rows(w_up[:, :, k * half:(k + 1) * half]) for k in range(2)], axis=2)
    keep_cols = jnp.broadcast_to(pattern[:, :, None], (factor_count, pattern.shape[1], BS)).reshape(
        factor_count, hidden_width
    )
    masked = (weights * keep_cols.astype(jnp.bfloat16)[:, None, :]).reshape(
        factor_count, BS, local_blocks, group_width
    )
    keep_f = keep_cols.astype(jnp.float32).reshape(factor_count, local_blocks, group_width)
    token_blocks = tokens.reshape(row_count, local_blocks, BS)
    gathered = []
    for factor in range(factor_count):
        stride = stride_of(factor)
        if stride < local_blocks:
            gathered.append(flip_blocks(token_blocks, stride))
        else:
            bit_number = (stride // local_blocks).bit_length() - 1
            partner = partner_2(tokens, "fly", bit_number)
            gathered.append(partner.reshape(row_count, local_blocks, BS))
    reads = jnp.stack(gathered, axis=2)
    contribs = []
    products = []
    for group in range(local_blocks):
        lhs = reads[:, group].reshape(row_count, factor_count * BS)
        rhs = masked[:, :, group, :].reshape(factor_count * BS, group_width)
        pre_act = jnp.dot(lhs, rhs, preferred_element_type=jnp.float32)
        squash = jax.nn.sigmoid(pre_act)
        derivative = squash * (1.0 + pre_act * (1.0 - squash))
        grad_pre = (hidden_grad[:, group * group_width:(group + 1) * group_width].astype(jnp.float32) * derivative).astype(
            jnp.bfloat16
        )
        contribs.append(
            lax.dot_general(grad_pre, rhs, (((1,), (1,)), ((), ())), preferred_element_type=jnp.float32).reshape(
                row_count, factor_count, BS
            )
        )
        cols = reads[:, group].reshape(row_count, factor_count, zl, xx, own).transpose(0, 3, 2, 4, 1)
        products.append(
            lax.dot_general(
                cols.reshape(row_count, BS * factor_count), grad_pre, (((0,), (0,)), ((), ())),
                preferred_element_type=jnp.float32,
            ).reshape(xx, zl, own, factor_count, group_width)
        )
    contrib_all = jnp.stack(contribs, axis=1)
    input_total = jnp.zeros((row_count, local_blocks, BS), jnp.float32)
    for factor in range(factor_count):
        stride = stride_of(factor)
        contrib = contrib_all[:, :, factor, :]
        if stride < local_blocks:
            input_total = input_total + flip_blocks(contrib, stride)
        else:
            bit_number = (stride // local_blocks).bit_length() - 1
            returned = partner_2(contrib.reshape(row_count, local_width), "fly", bit_number)
            input_total = input_total + returned.reshape(row_count, local_blocks, BS)
    input_grad = input_total.reshape(row_count, local_width).astype(jnp.bfloat16)
    terms = jnp.stack(products, axis=4) * keep_f[None, None, None]
    summed = scatter_rows(terms.reshape(xx, zl, own, factor_count, hidden_width).astype(jnp.bfloat16))
    weight_grad = summed * (1.0 / (zl * xx))
    return (input_grad, weight_grad)


def split_mesh(mesh):
    devices = mesh.devices
    xs = sorted({d.coords[0] for d in devices[:, 0]})
    cols = len(xs)
    return Mesh(devices.reshape(devices.shape[0] // cols, cols, devices.shape[1]), (ROWS, COLS, "fly"))


def solution(mesh):
    grid = split_mesh(mesh)
    return jax.shard_map(
        layer,
        mesh=grid,
        in_specs=(P(DP, "fly"), P(DP, "fly"), P(None, DP, "fly"), P(None, "fly")),
        out_specs=(P(DP, "fly"), P(None, DP, "fly")),
        check_vma=False,
    )
```

```python
import jax
import jax.numpy as jnp
from jax import lax
from jax.sharding import Mesh
from jax.sharding import PartitionSpec as P


BS = 256
ROWS = "zl"
COLS = "xx"
DP = (ROWS, COLS)


def partner_2(block, axis, bit):
    count = lax.axis_size(axis)
    route = []
    for low in range(count):
        high = low | 1 << bit
        if high != low and high < count:
            route += [(low, high), (high, low)]
    return lax.ppermute(block, axis, route)


def flip_blocks(values, stride):
    if stride == 0:
        return values
    row_count, block_count, inner_size = values.shape
    shaped = values.reshape(row_count, block_count // (2 * stride), 2, stride, inner_size)
    return shaped[:, :, ::-1].reshape(row_count, block_count, inner_size)


def stride_of(factor):
    return 0 if factor == 0 else 2 ** (factor - 1)


def gather_line(block, axis):
    count = lax.axis_size(axis)
    bits = count.bit_length() - 1
    assert 1 << bits == count
    place = lax.axis_index(axis)
    held = block[None]
    for step in range(bits):
        dist = count >> (step + 1)
        got = lax.ppermute(held, axis, [(i, i ^ dist) for i in range(count)])
        upper = (place & dist) != 0
        held = jnp.where(upper, jnp.stack([got, held]), jnp.stack([held, got]))
    order = tuple(reversed(range(bits))) + tuple(range(bits, bits + block.ndim))
    return held.reshape((2,) * bits + block.shape).transpose(order).reshape((count,) + block.shape)


def gather_rows(w_up):
    factor_count, own, width = w_up.shape
    zl = lax.axis_size(ROWS)
    xx = lax.axis_size(COLS)
    by_row = gather_line(w_up, ROWS)
    copies = jnp.broadcast_to(by_row[None], (xx, zl, factor_count, own, width))
    both = lax.all_to_all(copies, COLS, 0, 0, tiled=True)
    return both.transpose(2, 1, 0, 3, 4).reshape(factor_count, zl * xx * own, width)


def scatter_rows(terms):
    got = lax.all_to_all(terms, COLS, 0, 0, tiled=True)
    part = got.astype(jnp.float32).sum(0)
    got = lax.all_to_all(part.astype(jnp.bfloat16), ROWS, 0, 0, tiled=True)
    part = got.astype(jnp.float32).sum(0)
    return part.transpose(1, 0, 2)


def chunk_math(reads, weights, hidden_grad, keep_cols, group):
    row_count = reads.shape[0]
    factor_count, _, group_width = weights.shape
    zl = lax.axis_size(ROWS)
    xx = lax.axis_size(COLS)
    own = BS // (zl * xx)
    rhs = (weights * keep_cols[:, group].astype(jnp.bfloat16)[:, None, :]).reshape(factor_count * BS, group_width)
    lhs = reads.reshape(row_count, factor_count * BS)
    pre_act = jnp.dot(lhs, rhs, preferred_element_type=jnp.float32)
    squash = jax.nn.sigmoid(pre_act)
    derivative = squash * (1.0 + pre_act * (1.0 - squash))
    grad_pre = (hidden_grad[:, group * group_width:(group + 1) * group_width].astype(jnp.float32) * derivative).astype(
        jnp.bfloat16
    )
    contrib = lax.dot_general(grad_pre, rhs, (((1,), (1,)), ((), ())), preferred_element_type=jnp.float32).reshape(
        row_count, factor_count, BS
    )
    cols = reads.reshape(row_count, factor_count, zl, xx, own).transpose(0, 3, 2, 4, 1)
    product = lax.dot_general(
        cols.reshape(row_count, BS * factor_count), grad_pre, (((0,), (0,)), ((), ())),
        preferred_element_type=jnp.float32,
    ).reshape(xx, zl, own, factor_count, group_width)
    product = product * keep_cols[:, group].astype(jnp.float32)[None, None, None]
    return grad_pre, contrib, product.astype(jnp.bfloat16)


def layer(tokens, hidden_grad, w_up, pattern):
    row_count, local_width = tokens.shape
    factor_count = w_up.shape[0]
    hidden_width = hidden_grad.shape[1]
    local_blocks = local_width // BS
    group_width = hidden_width // local_blocks
    zl = lax.axis_size(ROWS)
    xx = lax.axis_size(COLS)
    keep_cols = jnp.broadcast_to(pattern[:, :, None], (factor_count, pattern.shape[1], BS)).reshape(
        factor_count, local_blocks, group_width
    )
    token_blocks = tokens.reshape(row_count, local_blocks, BS)
    gathered = []
    for factor in range(factor_count):
        stride = stride_of(factor)
        if stride < local_blocks:
            gathered.append(flip_blocks(token_blocks, stride))
        else:
            bit_number = (stride // local_blocks).bit_length() - 1
            partner = partner_2(tokens, "fly", bit_number)
            gathered.append(partner.reshape(row_count, local_blocks, BS))
    reads = jnp.stack(gathered, axis=2)
    contribs = []
    sums = []
    for group in range(local_blocks):
        weights = gather_rows(w_up[:, :, group * group_width:(group + 1) * group_width])
        _, contrib, product = chunk_math(reads[:, group], weights, hidden_grad, keep_cols, group)
        contribs.append(contrib)
        sums.append(product)
    contrib_all = jnp.stack(contribs, axis=1)
    input_total = jnp.zeros((row_count, local_blocks, BS), jnp.float32)
    for factor in range(factor_count):
        stride = stride_of(factor)
        contrib = contrib_all[:, :, factor, :]
        if stride < local_blocks:
            input_total = input_total + flip_blocks(contrib, stride)
        else:
            bit_number = (stride // local_blocks).bit_length() - 1
            returned = partner_2(contrib.reshape(row_count, local_width), "fly", bit_number)
            input_total = input_total + returned.reshape(row_count, local_blocks, BS)
    input_grad = input_total.reshape(row_count, local_width).astype(jnp.bfloat16)
    weight_grad = scatter_rows(jnp.concatenate(sums, axis=4)) * (1.0 / (zl * xx))
    return (input_grad, weight_grad)


def split_mesh(mesh):
    devices = mesh.devices
    xs = sorted({d.coords[0] for d in devices[:, 0]})
    cols = len(xs)
    return Mesh(devices.reshape(devices.shape[0] // cols, cols, devices.shape[1]), (ROWS, COLS, "fly"))


def solution(mesh):
    grid = split_mesh(mesh)
    return jax.shard_map(
        layer,
        mesh=grid,
        in_specs=(P(DP, "fly"), P(DP, "fly"), P(None, DP, "fly"), P(None, "fly")),
        out_specs=(P(DP, "fly"), P(None, DP, "fly")),
        check_vma=False,
    )
```

```python
import jax
import jax.numpy as jnp
from jax import lax
from jax.sharding import Mesh
from jax.sharding import PartitionSpec as P


BS = 256
HALF = "zh"
QUARTER = "zq"
ROWS = (HALF, QUARTER)
COLS = "xx"
DP = (HALF, QUARTER, COLS)


def partner_2(block, axis, bit):
    count = lax.axis_size(axis)
    route = []
    for low in range(count):
        high = low | 1 << bit
        if high != low and high < count:
            route += [(low, high), (high, low)]
    return lax.ppermute(block, axis, route)


def flip_blocks(values, stride):
    if stride == 0:
        return values
    row_count, block_count, inner_size = values.shape
    shaped = values.reshape(row_count, block_count // (2 * stride), 2, stride, inner_size)
    return shaped[:, :, ::-1].reshape(row_count, block_count, inner_size)


def stride_of(factor):
    return 0 if factor == 0 else 2 ** (factor - 1)


def gather_line(block, axis):
    count = lax.axis_size(axis)
    bits = count.bit_length() - 1
    assert 1 << bits == count
    place = lax.axis_index(axis)
    held = block[None]
    for step in range(bits):
        dist = count >> (step + 1)
        got = lax.ppermute(held, axis, [(i, i ^ dist) for i in range(count)])
        upper = (place & dist) != 0
        held = jnp.where(upper, jnp.stack([got, held]), jnp.stack([held, got]))
    order = tuple(reversed(range(bits))) + tuple(range(bits, bits + block.ndim))
    return held.reshape((2,) * bits + block.shape).transpose(order).reshape((count,) + block.shape)


def gather_rows(w_up):
    factor_count, own, width = w_up.shape
    zl = lax.axis_size(ROWS)
    xx = lax.axis_size(COLS)
    by_row = gather_line(w_up, ROWS)
    copies = jnp.broadcast_to(by_row[None], (xx, zl, factor_count, own, width))
    both = lax.all_to_all(copies, COLS, 0, 0, tiled=True)
    return both.transpose(2, 1, 0, 3, 4).reshape(factor_count, zl * xx * own, width)


def ring_scatter(terms, axis):
    count = lax.axis_size(axis)
    assert count == 4
    place = lax.axis_index(axis)
    half = terms.shape[-1] // 2

    def chunk(shift):
        return lax.dynamic_index_in_dim(terms, (place + shift) % count, 0, keepdims=False)

    right = [(i, (i + 1) % count) for i in range(count)]
    left = [(i, (i - 1) % count) for i in range(count)]
    opposite = chunk(2).astype(jnp.bfloat16)
    from_left = lax.ppermute(opposite[..., :half], axis, right).astype(jnp.float32)
    from_right = lax.ppermute(opposite[..., half:], axis, left).astype(jnp.float32)
    to_right = chunk(1)
    to_right = jnp.concatenate([to_right[..., :half] + from_left, to_right[..., half:]], axis=-1)
    to_left = chunk(3)
    to_left = jnp.concatenate([to_left[..., :half], to_left[..., half:] + from_right], axis=-1)
    got_left = lax.ppermute(to_right.astype(jnp.bfloat16), axis, right)
    got_right = lax.ppermute(to_left.astype(jnp.bfloat16), axis, left)
    own = chunk(0).astype(jnp.bfloat16).astype(jnp.float32)
    return own + got_left.astype(jnp.float32) + got_right.astype(jnp.float32)


def scatter_rows(terms):
    _, zl, own, factor_count, width = terms.shape
    halves = lax.axis_size(HALF)
    part = ring_scatter(terms, COLS)
    part = part.reshape(halves, zl // halves, own, factor_count, width)
    got = lax.all_to_all(part.transpose(1, 0, 2, 3, 4).astype(jnp.bfloat16), QUARTER, 0, 0, tiled=True)
    part = got.astype(jnp.float32).sum(0)
    got = lax.all_to_all(part.astype(jnp.bfloat16), HALF, 0, 0, tiled=True)
    part = got.astype(jnp.float32).sum(0)
    return part.transpose(1, 0, 2)


def chunk_math(reads, weights, hidden_grad, keep_cols, group):
    row_count = reads.shape[0]
    factor_count, _, group_width = weights.shape
    zl = lax.axis_size(ROWS)
    xx = lax.axis_size(COLS)
    own = BS // (zl * xx)
    rhs = (weights * keep_cols[:, group].astype(jnp.bfloat16)[:, None, :]).reshape(factor_count * BS, group_width)
    lhs = reads.reshape(row_count, factor_count * BS)
    pre_act = jnp.dot(lhs, rhs, preferred_element_type=jnp.float32)
    squash = jax.nn.sigmoid(pre_act)
    derivative = squash * (1.0 + pre_act * (1.0 - squash))
    grad_pre = (hidden_grad[:, group * group_width:(group + 1) * group_width].astype(jnp.float32) * derivative).astype(
        jnp.bfloat16
    )
    contrib = lax.dot_general(grad_pre, rhs, (((1,), (1,)), ((), ())), preferred_element_type=jnp.float32).reshape(
        row_count, factor_count, BS
    )
    cols = reads.reshape(row_count, factor_count, zl, xx, own).transpose(0, 3, 2, 4, 1)
    product = lax.dot_general(
        cols.reshape(row_count, BS * factor_count), grad_pre, (((0,), (0,)), ((), ())),
        preferred_element_type=jnp.float32,
    ).reshape(xx, zl, own, factor_count, group_width)
    product = product * keep_cols[:, group].astype(jnp.float32)[None, None, None]
    return grad_pre, contrib, product


def layer(tokens, hidden_grad, w_up, pattern):
    row_count, local_width = tokens.shape
    factor_count = w_up.shape[0]
    hidden_width = hidden_grad.shape[1]
    local_blocks = local_width // BS
    group_width = hidden_width // local_blocks
    zl = lax.axis_size(ROWS)
    xx = lax.axis_size(COLS)
    keep_cols = jnp.broadcast_to(pattern[:, :, None], (factor_count, pattern.shape[1], BS)).reshape(
        factor_count, local_blocks, group_width
    )
    token_blocks = tokens.reshape(row_count, local_blocks, BS)
    gathered = []
    for factor in range(factor_count):
        stride = stride_of(factor)
        if stride < local_blocks:
            gathered.append(flip_blocks(token_blocks, stride))
        else:
            bit_number = (stride // local_blocks).bit_length() - 1
            partner = partner_2(tokens, "fly", bit_number)
            gathered.append(partner.reshape(row_count, local_blocks, BS))
    reads = jnp.stack(gathered, axis=2)
    contribs = []
    sums = []
    for group in range(local_blocks):
        weights = gather_rows(w_up[:, :, group * group_width:(group + 1) * group_width])
        _, contrib, product = chunk_math(reads[:, group], weights, hidden_grad, keep_cols, group)
        contribs.append(contrib)
        sums.append(product)
    contrib_all = jnp.stack(contribs, axis=1)
    input_total = jnp.zeros((row_count, local_blocks, BS), jnp.float32)
    for factor in range(factor_count):
        stride = stride_of(factor)
        contrib = contrib_all[:, :, factor, :]
        if stride < local_blocks:
            input_total = input_total + flip_blocks(contrib, stride)
        else:
            bit_number = (stride // local_blocks).bit_length() - 1
            returned = partner_2(contrib.reshape(row_count, local_width), "fly", bit_number)
            input_total = input_total + returned.reshape(row_count, local_blocks, BS)
    input_grad = input_total.reshape(row_count, local_width).astype(jnp.bfloat16)
    weight_grad = scatter_rows(jnp.concatenate(sums, axis=4)) * (1.0 / (zl * xx))
    return (input_grad, weight_grad)


def split_mesh(mesh):
    devices = mesh.devices
    xs = sorted({d.coords[0] for d in devices[:, 0]})
    cols = len(xs)
    lines = devices.shape[0] // cols
    return Mesh(devices.reshape(2, lines // 2, cols, devices.shape[1]), (HALF, QUARTER, COLS, "fly"))


def solution(mesh):
    grid = split_mesh(mesh)
    return jax.shard_map(
        layer,
        mesh=grid,
        in_specs=(P(DP, "fly"), P(DP, "fly"), P(None, DP, "fly"), P(None, "fly")),
        out_specs=(P(DP, "fly"), P(None, DP, "fly")),
        check_vma=False,
    )
```

```python
import jax
import jax.numpy as jnp
from jax import lax
from jax.sharding import Mesh
from jax.sharding import PartitionSpec as P


BS = 256
HALF = "zh"
QUARTER = "zq"
ROWS = (HALF, QUARTER)
COLS = "xx"
DP = (HALF, QUARTER, COLS)


def partner_2(block, axis, bit):
    count = lax.axis_size(axis)
    route = []
    for low in range(count):
        high = low | 1 << bit
        if high != low and high < count:
            route += [(low, high), (high, low)]
    return lax.ppermute(block, axis, route)


def flip_blocks(values, stride):
    if stride == 0:
        return values
    row_count, block_count, inner_size = values.shape
    shaped = values.reshape(row_count, block_count // (2 * stride), 2, stride, inner_size)
    return shaped[:, :, ::-1].reshape(row_count, block_count, inner_size)


def stride_of(factor):
    return 0 if factor == 0 else 2 ** (factor - 1)


def gather_line(block, axis):
    count = lax.axis_size(axis)
    bits = count.bit_length() - 1
    assert 1 << bits == count
    place = lax.axis_index(axis)
    held = block[None]
    for step in range(bits):
        dist = count >> (step + 1)
        got = lax.ppermute(held, axis, [(i, i ^ dist) for i in range(count)])
        upper = (place & dist) != 0
        held = jnp.where(upper, jnp.stack([got, held]), jnp.stack([held, got]))
    order = tuple(reversed(range(bits))) + tuple(range(bits, bits + block.ndim))
    return held.reshape((2,) * bits + block.shape).transpose(order).reshape((count,) + block.shape)


def gather_rows(w_up):
    factor_count, own, width = w_up.shape
    zl = lax.axis_size(ROWS)
    xx = lax.axis_size(COLS)
    by_row = gather_line(w_up, ROWS)
    copies = jnp.broadcast_to(by_row[None], (xx, zl, factor_count, own, width))
    both = lax.all_to_all(copies, COLS, 0, 0, tiled=True)
    return both.transpose(2, 1, 0, 3, 4).reshape(factor_count, zl * xx * own, width)


def scatter_rows(terms):
    _, zl, own, factor_count, width = terms.shape
    halves = lax.axis_size(HALF)
    got = lax.all_to_all(terms, COLS, 0, 0, tiled=True)
    part = got.astype(jnp.float32).sum(0).reshape(halves, zl // halves, own, factor_count, width)
    got = lax.all_to_all(part.transpose(1, 0, 2, 3, 4).astype(jnp.bfloat16), QUARTER, 0, 0, tiled=True)
    part = got.astype(jnp.float32).sum(0)
    got = lax.all_to_all(part.astype(jnp.bfloat16), HALF, 0, 0, tiled=True)
    part = got.astype(jnp.float32).sum(0)
    return part.transpose(1, 0, 2)


def chunk_math(reads, weights, hidden_grad, keep_cols, group):
    row_count = reads.shape[0]
    factor_count, _, group_width = weights.shape
    zl = lax.axis_size(ROWS)
    xx = lax.axis_size(COLS)
    own = BS // (zl * xx)
    rhs = (weights * keep_cols[:, group].astype(jnp.bfloat16)[:, None, :]).reshape(factor_count * BS, group_width)
    lhs = reads.reshape(row_count, factor_count * BS)
    pre_act = jnp.dot(lhs, rhs, preferred_element_type=jnp.float32)
    squash = jax.nn.sigmoid(pre_act)
    derivative = squash * (1.0 + pre_act * (1.0 - squash))
    grad_pre = (hidden_grad[:, group * group_width:(group + 1) * group_width].astype(jnp.float32) * derivative).astype(
        jnp.bfloat16
    )
    contrib = lax.dot_general(grad_pre, rhs, (((1,), (1,)), ((), ())), preferred_element_type=jnp.float32).reshape(
        row_count, factor_count, BS
    )
    cols = reads.reshape(row_count, factor_count, zl, xx, own).transpose(0, 3, 2, 4, 1)
    product = lax.dot_general(
        cols.reshape(row_count, BS * factor_count), grad_pre, (((0,), (0,)), ((), ())),
        preferred_element_type=jnp.float32,
    ).reshape(xx, zl, own, factor_count, group_width)
    product = product * keep_cols[:, group].astype(jnp.float32)[None, None, None]
    return grad_pre, contrib, product.astype(jnp.bfloat16)


def layer(tokens, hidden_grad, w_up, pattern):
    row_count, local_width = tokens.shape
    factor_count = w_up.shape[0]
    hidden_width = hidden_grad.shape[1]
    local_blocks = local_width // BS
    group_width = hidden_width // local_blocks
    zl = lax.axis_size(ROWS)
    xx = lax.axis_size(COLS)
    keep_cols = jnp.broadcast_to(pattern[:, :, None], (factor_count, pattern.shape[1], BS)).reshape(
        factor_count, local_blocks, group_width
    )
    token_blocks = tokens.reshape(row_count, local_blocks, BS)
    gathered = []
    for factor in range(factor_count):
        stride = stride_of(factor)
        if stride < local_blocks:
            gathered.append(flip_blocks(token_blocks, stride))
        else:
            bit_number = (stride // local_blocks).bit_length() - 1
            partner = partner_2(tokens, "fly", bit_number)
            gathered.append(partner.reshape(row_count, local_blocks, BS))
    reads = jnp.stack(gathered, axis=2)
    contribs = []
    sums = []
    for group in range(local_blocks):
        weights = gather_rows(w_up[:, :, group * group_width:(group + 1) * group_width])
        _, contrib, product = chunk_math(reads[:, group], weights, hidden_grad, keep_cols, group)
        contribs.append(contrib)
        sums.append(product)
    contrib_all = jnp.stack(contribs, axis=1)
    input_total = jnp.zeros((row_count, local_blocks, BS), jnp.float32)
    for factor in range(factor_count):
        stride = stride_of(factor)
        contrib = contrib_all[:, :, factor, :]
        if stride < local_blocks:
            input_total = input_total + flip_blocks(contrib, stride)
        else:
            bit_number = (stride // local_blocks).bit_length() - 1
            returned = partner_2(contrib.reshape(row_count, local_width).astype(jnp.bfloat16), "fly", bit_number)
            input_total = input_total + returned.astype(jnp.float32).reshape(row_count, local_blocks, BS)
    input_grad = input_total.reshape(row_count, local_width).astype(jnp.bfloat16)
    weight_grad = scatter_rows(jnp.concatenate(sums, axis=4)) * (1.0 / (zl * xx))
    return (input_grad, weight_grad)


def split_mesh(mesh):
    devices = mesh.devices
    xs = sorted({d.coords[0] for d in devices[:, 0]})
    cols = len(xs)
    lines = devices.shape[0] // cols
    return Mesh(devices.reshape(2, lines // 2, cols, devices.shape[1]), (HALF, QUARTER, COLS, "fly"))


def solution(mesh):
    grid = split_mesh(mesh)
    return jax.shard_map(
        layer,
        mesh=grid,
        in_specs=(P(DP, "fly"), P(DP, "fly"), P(None, DP, "fly"), P(None, "fly")),
        out_specs=(P(DP, "fly"), P(None, DP, "fly")),
        check_vma=False,
    )
```

```python
import jax
import jax.numpy as jnp
from jax import lax
from jax.sharding import Mesh
from jax.sharding import PartitionSpec as P


BS = 256
HALF = "zh"
QUARTER = "zq"
ROWS = (HALF, QUARTER)
COLS = "xx"
DP = (HALF, QUARTER, COLS)


def partner_2(block, axis, bit):
    count = lax.axis_size(axis)
    route = []
    for low in range(count):
        high = low | 1 << bit
        if high != low and high < count:
            route += [(low, high), (high, low)]
    return lax.ppermute(block, axis, route)


def flip_blocks(values, stride):
    if stride == 0:
        return values
    row_count, block_count, inner_size = values.shape
    shaped = values.reshape(row_count, block_count // (2 * stride), 2, stride, inner_size)
    return shaped[:, :, ::-1].reshape(row_count, block_count, inner_size)


def stride_of(factor):
    return 0 if factor == 0 else 2 ** (factor - 1)


def gather_line(block, axis):
    count = lax.axis_size(axis)
    bits = count.bit_length() - 1
    assert 1 << bits == count
    place = lax.axis_index(axis)
    held = block[None]
    for step in range(bits):
        dist = count >> (step + 1)
        got = lax.ppermute(held, axis, [(i, i ^ dist) for i in range(count)])
        upper = (place & dist) != 0
        held = jnp.where(upper, jnp.stack([got, held]), jnp.stack([held, got]))
    order = tuple(reversed(range(bits))) + tuple(range(bits, bits + block.ndim))
    return held.reshape((2,) * bits + block.shape).transpose(order).reshape((count,) + block.shape)


def gather_rows(w_up):
    factor_count, own, width = w_up.shape
    zl = lax.axis_size(ROWS)
    xx = lax.axis_size(COLS)
    by_row = gather_line(w_up, ROWS)
    copies = jnp.broadcast_to(by_row[None], (xx, zl, factor_count, own, width))
    both = lax.all_to_all(copies, COLS, 0, 0, tiled=True)
    return both.transpose(2, 1, 0, 3, 4).reshape(factor_count, zl * xx * own, width)


def scatter_rows(terms):
    _, zl, own, factor_count, width = terms.shape
    halves = lax.axis_size(HALF)
    got = lax.all_to_all(terms, COLS, 0, 0, tiled=True)
    part = got.astype(jnp.float32).sum(0).reshape(halves, zl // halves, own, factor_count, width)
    got = lax.all_to_all(part.transpose(1, 0, 2, 3, 4).astype(jnp.bfloat16), QUARTER, 0, 0, tiled=True)
    part = got.astype(jnp.float32).sum(0)
    sent = part.astype(jnp.bfloat16)
    place = lax.axis_index(HALF)
    got = lax.ppermute(lax.dynamic_index_in_dim(sent, 1 - place, 0, keepdims=False), HALF, [(0, 1), (1, 0)])
    part = lax.dynamic_index_in_dim(sent, place, 0, keepdims=False).astype(jnp.float32) + got.astype(jnp.float32)
    return part.transpose(1, 0, 2)


def chunk_math(reads, weights, hidden_grad, keep_cols, group):
    row_count = reads.shape[0]
    factor_count, _, group_width = weights.shape
    zl = lax.axis_size(ROWS)
    xx = lax.axis_size(COLS)
    own = BS // (zl * xx)
    rhs = (weights * keep_cols[:, group].astype(jnp.bfloat16)[:, None, :]).reshape(factor_count * BS, group_width)
    lhs = reads.reshape(row_count, factor_count * BS)
    pre_act = jnp.dot(lhs, rhs, preferred_element_type=jnp.float32)
    squash = jax.nn.sigmoid(pre_act)
    derivative = squash * (1.0 + pre_act * (1.0 - squash))
    grad_pre = (hidden_grad[:, group * group_width:(group + 1) * group_width].astype(jnp.float32) * derivative).astype(
        jnp.bfloat16
    )
    contrib = lax.dot_general(grad_pre, rhs, (((1,), (1,)), ((), ())), preferred_element_type=jnp.float32).reshape(
        row_count, factor_count, BS
    )
    cols = reads.reshape(row_count, factor_count, zl, xx, own).transpose(0, 3, 2, 4, 1)
    product = lax.dot_general(
        cols.reshape(row_count, BS * factor_count), grad_pre, (((0,), (0,)), ((), ())),
        preferred_element_type=jnp.float32,
    ).reshape(xx, zl, own, factor_count, group_width)
    product = product * keep_cols[:, group].astype(jnp.float32)[None, None, None]
    return grad_pre, contrib, product.astype(jnp.bfloat16)


def layer(tokens, hidden_grad, w_up, pattern):
    row_count, local_width = tokens.shape
    factor_count = w_up.shape[0]
    hidden_width = hidden_grad.shape[1]
    local_blocks = local_width // BS
    group_width = hidden_width // local_blocks
    zl = lax.axis_size(ROWS)
    xx = lax.axis_size(COLS)
    keep_cols = jnp.broadcast_to(pattern[:, :, None], (factor_count, pattern.shape[1], BS)).reshape(
        factor_count, local_blocks, group_width
    )
    token_blocks = tokens.reshape(row_count, local_blocks, BS)
    gathered = []
    for factor in range(factor_count):
        stride = stride_of(factor)
        if stride < local_blocks:
            gathered.append(flip_blocks(token_blocks, stride))
        else:
            bit_number = (stride // local_blocks).bit_length() - 1
            partner = partner_2(tokens, "fly", bit_number)
            gathered.append(partner.reshape(row_count, local_blocks, BS))
    reads = jnp.stack(gathered, axis=2)
    contribs = []
    sums = []
    for group in range(local_blocks):
        weights = gather_rows(w_up[:, :, group * group_width:(group + 1) * group_width])
        _, contrib, product = chunk_math(reads[:, group], weights, hidden_grad, keep_cols, group)
        contribs.append(contrib)
        sums.append(product)
    contrib_all = jnp.stack(contribs, axis=1)
    input_total = jnp.zeros((row_count, local_blocks, BS), jnp.float32)
    for factor in range(factor_count):
        stride = stride_of(factor)
        contrib = contrib_all[:, :, factor, :]
        if stride < local_blocks:
            input_total = input_total + flip_blocks(contrib, stride)
        else:
            bit_number = (stride // local_blocks).bit_length() - 1
            returned = partner_2(contrib.reshape(row_count, local_width).astype(jnp.bfloat16), "fly", bit_number)
            input_total = input_total + returned.astype(jnp.float32).reshape(row_count, local_blocks, BS)
    input_grad = input_total.reshape(row_count, local_width).astype(jnp.bfloat16)
    weight_grad = scatter_rows(jnp.concatenate(sums, axis=4)) * (1.0 / (zl * xx))
    return (input_grad, weight_grad)


def split_mesh(mesh):
    devices = mesh.devices
    xs = sorted({d.coords[0] for d in devices[:, 0]})
    cols = len(xs)
    lines = devices.shape[0] // cols
    return Mesh(devices.reshape(2, lines // 2, cols, devices.shape[1]), (HALF, QUARTER, COLS, "fly"))


def solution(mesh):
    grid = split_mesh(mesh)
    return jax.shard_map(
        layer,
        mesh=grid,
        in_specs=(P(DP, "fly"), P(DP, "fly"), P(None, DP, "fly"), P(None, "fly")),
        out_specs=(P(DP, "fly"), P(None, DP, "fly")),
        check_vma=False,
    )
```

```python
import jax
import jax.numpy as jnp
from jax import lax
from jax.sharding import Mesh
from jax.sharding import PartitionSpec as P


BS = 256
HALF = "zh"
QUARTER = "zq"
ROWS = (HALF, QUARTER)
COLS = "xx"
DP = (HALF, QUARTER, COLS)


def partner_2(block, axis, bit):
    count = lax.axis_size(axis)
    route = []
    for low in range(count):
        high = low | 1 << bit
        if high != low and high < count:
            route += [(low, high), (high, low)]
    return lax.ppermute(block, axis, route)


def flip_blocks(values, stride):
    if stride == 0:
        return values
    row_count, block_count, inner_size = values.shape
    shaped = values.reshape(row_count, block_count // (2 * stride), 2, stride, inner_size)
    return shaped[:, :, ::-1].reshape(row_count, block_count, inner_size)


def stride_of(factor):
    return 0 if factor == 0 else 2 ** (factor - 1)


def gather_line(block, axis):
    count = lax.axis_size(axis)
    bits = count.bit_length() - 1
    assert 1 << bits == count
    place = lax.axis_index(axis)
    held = block[None]
    for step in range(bits):
        dist = count >> (step + 1)
        got = lax.ppermute(held, axis, [(i, i ^ dist) for i in range(count)])
        upper = (place & dist) != 0
        held = jnp.where(upper, jnp.stack([got, held]), jnp.stack([held, got]))
    order = tuple(reversed(range(bits))) + tuple(range(bits, bits + block.ndim))
    return held.reshape((2,) * bits + block.shape).transpose(order).reshape((count,) + block.shape)


def gather_rows(w_up):
    factor_count, own, width = w_up.shape
    zl = lax.axis_size(ROWS)
    xx = lax.axis_size(COLS)
    by_row = gather_line(w_up, ROWS)
    copies = jnp.broadcast_to(by_row[None], (xx, zl, factor_count, own, width))
    both = lax.all_to_all(copies, COLS, 0, 0, tiled=True)
    return both.transpose(2, 1, 0, 3, 4).reshape(factor_count, zl * xx * own, width)


def scatter_rows(terms):
    _, zl, own, factor_count, width = terms.shape
    halves = lax.axis_size(HALF)
    got = lax.all_to_all(terms, COLS, 0, 0, tiled=True)
    part = got.astype(jnp.float32).sum(0).reshape(halves, zl // halves, own, factor_count, width)
    data = part.transpose(1, 0, 2, 3, 4).astype(jnp.bfloat16)
    count = lax.axis_size(QUARTER)
    at = lax.axis_index(QUARTER)
    part = lax.dynamic_index_in_dim(data, at, 0, keepdims=False).astype(jnp.float32)
    for step in range(1, count):
        got = lax.ppermute(
            lax.dynamic_index_in_dim(data, at ^ step, 0, keepdims=False), QUARTER, [(i, i ^ step) for i in range(count)]
        )
        part = part + got.astype(jnp.float32)
    sent = part.astype(jnp.bfloat16)
    place = lax.axis_index(HALF)
    got = lax.ppermute(lax.dynamic_index_in_dim(sent, 1 - place, 0, keepdims=False), HALF, [(0, 1), (1, 0)])
    part = lax.dynamic_index_in_dim(sent, place, 0, keepdims=False).astype(jnp.float32) + got.astype(jnp.float32)
    return part.transpose(1, 0, 2)


def chunk_math(reads, weights, hidden_grad, keep_cols, group):
    row_count = reads.shape[0]
    factor_count, _, group_width = weights.shape
    zl = lax.axis_size(ROWS)
    xx = lax.axis_size(COLS)
    own = BS // (zl * xx)
    rhs = (weights * keep_cols[:, group].astype(jnp.bfloat16)[:, None, :]).reshape(factor_count * BS, group_width)
    lhs = reads.reshape(row_count, factor_count * BS)
    pre_act = jnp.dot(lhs, rhs, preferred_element_type=jnp.float32)
    squash = jax.nn.sigmoid(pre_act)
    derivative = squash * (1.0 + pre_act * (1.0 - squash))
    grad_pre = (hidden_grad[:, group * group_width:(group + 1) * group_width].astype(jnp.float32) * derivative).astype(
        jnp.bfloat16
    )
    contrib = lax.dot_general(grad_pre, rhs, (((1,), (1,)), ((), ())), preferred_element_type=jnp.float32).reshape(
        row_count, factor_count, BS
    )
    cols = reads.reshape(row_count, factor_count, zl, xx, own).transpose(0, 3, 2, 4, 1)
    product = lax.dot_general(
        cols.reshape(row_count, BS * factor_count), grad_pre, (((0,), (0,)), ((), ())),
        preferred_element_type=jnp.float32,
    ).reshape(xx, zl, own, factor_count, group_width)
    product = product * keep_cols[:, group].astype(jnp.float32)[None, None, None]
    return grad_pre, contrib, product.astype(jnp.bfloat16)


def layer(tokens, hidden_grad, w_up, pattern):
    row_count, local_width = tokens.shape
    factor_count = w_up.shape[0]
    hidden_width = hidden_grad.shape[1]
    local_blocks = local_width // BS
    group_width = hidden_width // local_blocks
    zl = lax.axis_size(ROWS)
    xx = lax.axis_size(COLS)
    keep_cols = jnp.broadcast_to(pattern[:, :, None], (factor_count, pattern.shape[1], BS)).reshape(
        factor_count, local_blocks, group_width
    )
    token_blocks = tokens.reshape(row_count, local_blocks, BS)
    gathered = []
    for factor in range(factor_count):
        stride = stride_of(factor)
        if stride < local_blocks:
            gathered.append(flip_blocks(token_blocks, stride))
        else:
            bit_number = (stride // local_blocks).bit_length() - 1
            partner = partner_2(tokens, "fly", bit_number)
            gathered.append(partner.reshape(row_count, local_blocks, BS))
    reads = jnp.stack(gathered, axis=2)
    contribs = []
    sums = []
    for group in range(local_blocks):
        weights = gather_rows(w_up[:, :, group * group_width:(group + 1) * group_width])
        _, contrib, product = chunk_math(reads[:, group], weights, hidden_grad, keep_cols, group)
        contribs.append(contrib)
        sums.append(product)
    contrib_all = jnp.stack(contribs, axis=1)
    input_total = jnp.zeros((row_count, local_blocks, BS), jnp.float32)
    for factor in range(factor_count):
        stride = stride_of(factor)
        contrib = contrib_all[:, :, factor, :]
        if stride < local_blocks:
            input_total = input_total + flip_blocks(contrib, stride)
        else:
            bit_number = (stride // local_blocks).bit_length() - 1
            returned = partner_2(contrib.reshape(row_count, local_width).astype(jnp.bfloat16), "fly", bit_number)
            input_total = input_total + returned.astype(jnp.float32).reshape(row_count, local_blocks, BS)
    input_grad = input_total.reshape(row_count, local_width).astype(jnp.bfloat16)
    weight_grad = scatter_rows(jnp.concatenate(sums, axis=4)) * (1.0 / (zl * xx))
    return (input_grad, weight_grad)


def split_mesh(mesh):
    devices = mesh.devices
    xs = sorted({d.coords[0] for d in devices[:, 0]})
    cols = len(xs)
    lines = devices.shape[0] // cols
    return Mesh(devices.reshape(2, lines // 2, cols, devices.shape[1]), (HALF, QUARTER, COLS, "fly"))


def solution(mesh):
    grid = split_mesh(mesh)
    return jax.shard_map(
        layer,
        mesh=grid,
        in_specs=(P(DP, "fly"), P(DP, "fly"), P(None, DP, "fly"), P(None, "fly")),
        out_specs=(P(DP, "fly"), P(None, DP, "fly")),
        check_vma=False,
    )
```

```python
import jax
import jax.numpy as jnp
from jax import lax
from jax.sharding import Mesh
from jax.sharding import PartitionSpec as P


BS = 256
HALF = "zh"
QUARTER = "zq"
ROWS = (HALF, QUARTER)
COLS = "xx"
DP = (HALF, QUARTER, COLS)


def partner_2(block, axis, bit):
    count = lax.axis_size(axis)
    route = []
    for low in range(count):
        high = low | 1 << bit
        if high != low and high < count:
            route += [(low, high), (high, low)]
    return lax.ppermute(block, axis, route)


def flip_blocks(values, stride):
    if stride == 0:
        return values
    row_count, block_count, inner_size = values.shape
    shaped = values.reshape(row_count, block_count // (2 * stride), 2, stride, inner_size)
    return shaped[:, :, ::-1].reshape(row_count, block_count, inner_size)


def stride_of(factor):
    return 0 if factor == 0 else 2 ** (factor - 1)


def gather_line(block, axis):
    count = lax.axis_size(axis)
    bits = count.bit_length() - 1
    assert 1 << bits == count
    place = lax.axis_index(axis)
    held = block[None]
    for step in range(bits):
        dist = count >> (step + 1)
        got = lax.ppermute(held, axis, [(i, i ^ dist) for i in range(count)])
        upper = (place & dist) != 0
        held = jnp.where(upper, jnp.stack([got, held]), jnp.stack([held, got]))
    order = tuple(reversed(range(bits))) + tuple(range(bits, bits + block.ndim))
    return held.reshape((2,) * bits + block.shape).transpose(order).reshape((count,) + block.shape)


def gather_rows(w_up):
    factor_count, own, width = w_up.shape
    zl = lax.axis_size(ROWS)
    xx = lax.axis_size(COLS)
    by_row = gather_line(w_up, ROWS)
    copies = jnp.broadcast_to(by_row[None], (xx, zl, factor_count, own, width))
    both = lax.all_to_all(copies, COLS, 0, 0, tiled=True)
    return both.transpose(2, 1, 0, 3, 4).reshape(factor_count, zl * xx * own, width)


def scatter_rows(terms):
    _, zl, own, factor_count, width = terms.shape
    halves = lax.axis_size(HALF)
    ring = lax.axis_size(COLS)
    me = lax.axis_index(COLS)
    part = lax.dynamic_index_in_dim(terms, me, 0, keepdims=False).astype(jnp.float32)
    for step in range(1, ring):
        got = lax.ppermute(
            lax.dynamic_index_in_dim(terms, me ^ step, 0, keepdims=False), COLS, [(i, i ^ step) for i in range(ring)]
        )
        part = part + got.astype(jnp.float32)
    part = part.reshape(halves, zl // halves, own, factor_count, width)
    data = part.transpose(1, 0, 2, 3, 4).astype(jnp.bfloat16)
    count = lax.axis_size(QUARTER)
    at = lax.axis_index(QUARTER)
    part = lax.dynamic_index_in_dim(data, at, 0, keepdims=False).astype(jnp.float32)
    for step in range(1, count):
        got = lax.ppermute(
            lax.dynamic_index_in_dim(data, at ^ step, 0, keepdims=False), QUARTER, [(i, i ^ step) for i in range(count)]
        )
        part = part + got.astype(jnp.float32)
    sent = part.astype(jnp.bfloat16)
    place = lax.axis_index(HALF)
    got = lax.ppermute(lax.dynamic_index_in_dim(sent, 1 - place, 0, keepdims=False), HALF, [(0, 1), (1, 0)])
    part = lax.dynamic_index_in_dim(sent, place, 0, keepdims=False).astype(jnp.float32) + got.astype(jnp.float32)
    return part.transpose(1, 0, 2)


def chunk_math(reads, weights, hidden_grad, keep_cols, group):
    row_count = reads.shape[0]
    factor_count, _, group_width = weights.shape
    zl = lax.axis_size(ROWS)
    xx = lax.axis_size(COLS)
    own = BS // (zl * xx)
    rhs = (weights * keep_cols[:, group].astype(jnp.bfloat16)[:, None, :]).reshape(factor_count * BS, group_width)
    lhs = reads.reshape(row_count, factor_count * BS)
    pre_act = jnp.dot(lhs, rhs, preferred_element_type=jnp.float32)
    squash = jax.nn.sigmoid(pre_act)
    derivative = squash * (1.0 + pre_act * (1.0 - squash))
    grad_pre = (hidden_grad[:, group * group_width:(group + 1) * group_width].astype(jnp.float32) * derivative).astype(
        jnp.bfloat16
    )
    contrib = lax.dot_general(grad_pre, rhs, (((1,), (1,)), ((), ())), preferred_element_type=jnp.float32).reshape(
        row_count, factor_count, BS
    )
    cols = reads.reshape(row_count, factor_count, zl, xx, own).transpose(0, 3, 2, 4, 1)
    product = lax.dot_general(
        cols.reshape(row_count, BS * factor_count), grad_pre, (((0,), (0,)), ((), ())),
        preferred_element_type=jnp.float32,
    ).reshape(xx, zl, own, factor_count, group_width)
    product = product * keep_cols[:, group].astype(jnp.float32)[None, None, None]
    return grad_pre, contrib, product.astype(jnp.bfloat16)


def layer(tokens, hidden_grad, w_up, pattern):
    row_count, local_width = tokens.shape
    factor_count = w_up.shape[0]
    hidden_width = hidden_grad.shape[1]
    local_blocks = local_width // BS
    group_width = hidden_width // local_blocks
    zl = lax.axis_size(ROWS)
    xx = lax.axis_size(COLS)
    keep_cols = jnp.broadcast_to(pattern[:, :, None], (factor_count, pattern.shape[1], BS)).reshape(
        factor_count, local_blocks, group_width
    )
    token_blocks = tokens.reshape(row_count, local_blocks, BS)
    gathered = []
    for factor in range(factor_count):
        stride = stride_of(factor)
        if stride < local_blocks:
            gathered.append(flip_blocks(token_blocks, stride))
        else:
            bit_number = (stride // local_blocks).bit_length() - 1
            partner = partner_2(tokens, "fly", bit_number)
            gathered.append(partner.reshape(row_count, local_blocks, BS))
    reads = jnp.stack(gathered, axis=2)
    contribs = []
    sums = []
    for group in range(local_blocks):
        weights = gather_rows(w_up[:, :, group * group_width:(group + 1) * group_width])
        _, contrib, product = chunk_math(reads[:, group], weights, hidden_grad, keep_cols, group)
        contribs.append(contrib)
        sums.append(product)
    contrib_all = jnp.stack(contribs, axis=1)
    input_total = jnp.zeros((row_count, local_blocks, BS), jnp.float32)
    for factor in range(factor_count):
        stride = stride_of(factor)
        contrib = contrib_all[:, :, factor, :]
        if stride < local_blocks:
            input_total = input_total + flip_blocks(contrib, stride)
        else:
            bit_number = (stride // local_blocks).bit_length() - 1
            returned = partner_2(contrib.reshape(row_count, local_width).astype(jnp.bfloat16), "fly", bit_number)
            input_total = input_total + returned.astype(jnp.float32).reshape(row_count, local_blocks, BS)
    input_grad = input_total.reshape(row_count, local_width).astype(jnp.bfloat16)
    weight_grad = scatter_rows(jnp.concatenate(sums, axis=4)) * (1.0 / (zl * xx))
    return (input_grad, weight_grad)


def split_mesh(mesh):
    devices = mesh.devices
    xs = sorted({d.coords[0] for d in devices[:, 0]})
    cols = len(xs)
    lines = devices.shape[0] // cols
    return Mesh(devices.reshape(2, lines // 2, cols, devices.shape[1]), (HALF, QUARTER, COLS, "fly"))


def solution(mesh):
    grid = split_mesh(mesh)
    return jax.shard_map(
        layer,
        mesh=grid,
        in_specs=(P(DP, "fly"), P(DP, "fly"), P(None, DP, "fly"), P(None, "fly")),
        out_specs=(P(DP, "fly"), P(None, DP, "fly")),
        check_vma=False,
    )
```
